1024 devices in a mesh: gx: 16 (over y, core), gy: 64 (over z, x).
Axes of the slice: x: 4, y: 8, z: 16, core: 2. Of those that a mesh axis runs over, the one named last changes fastest.
Arguments:
- pressure_init: float32 [256, 2048, 128], P('gx', 'gy'), may hold values from -6 to 6
- source: float32 [256, 2048, 128], P('gx', 'gy'), may hold values from -6 to 6
- permeability: float32 [256, 2048, 128], P('gx', 'gy'), may hold values from 0.1 to 10
Outputs:
- pressure: float32 [256, 2048, 128], P('gx', 'gy')
- correction_mid: float32 [128, 1024, 128], P('gx', 'gy')
- correction_coarse: float32 [64, 512, 128], P('gx', 'gy')
The draws below stay inside these ranges and needn't reach their ends.
All inputs are finite; a program needn't handle non-finite values.
Results may differ from the reference program's by a relative error of at most 0.0003.
Values sent between devices are 32-bit elements; how exact they have to be, the bound alone decides.
No kernel may reach another device: no remote copies, remote signals or barrier semaphores. Data moves between devices by JAX's collectives and lax.ppermute only.
A program may use at most 32 MiB of HBM per device.

```python
import math
import jax
import jax.numpy as jnp

NZ = 128
SWEEPS = 2
COARSE = 4
NX = 256
NY = 2048


def steps_of(key, extent, shards, low, largest):
    def one(dim, blocks):
        draws = jax.random.uniform(jax.random.fold_in(jax.random.fold_in(key, 6), dim), (blocks,), jnp.float32, low / len(shards), largest / len(shards))
        return jnp.repeat(jnp.exp(draws), extent[dim] // blocks).reshape((-1,) + (1,) * (len(extent) - dim - 1))

    level = one(*shards[0])
    for cut in shards[1:]:
        level = level * one(*cut)
    return level


def scatter_about(own_key, extent, width, bound, pieces=(), dtype=jnp.bfloat16):
    result = width * jax.random.normal(own_key, extent, jnp.float32)
    if pieces:
        result = result * steps_of(own_key, extent, pieces, -0.22, 0.18)
    return jnp.clip(result, -bound, bound).astype(dtype)


def setup_inputs(seed: int = 0) -> dict:
    streams_of = jax.random.split(jax.random.key(seed), 4)
    return {
        "pressure_init": scatter_about(streams_of[0], (NX, NY, NZ), 1.0, 6.0, ((0, 16), (1, 64)), jnp.float32),
        "source": scatter_about(streams_of[1], (NX, NY, NZ), 1.0, 6.0, ((0, 16), (1, 64)), jnp.float32),
        "permeability": jnp.clip(jnp.exp(math.log(10.0) - 4.6051702 * jax.random.uniform(streams_of[2], (NX, NY, NZ), jnp.float32) ** steps_of(streams_of[2], (NX, NY, NZ), ((0, 16), (1, 64)), -0.2, 0.2)), 0.1, 10.0),
    }


STORE = 0.1
OMEGA = 0.8


def harmonic(first, second):
    total = first + second
    return 2.0 * first * second / jnp.where(total > 0, total, 1.0)


def widths(axis, low):
    pads = [(0, 0), (0, 0), (0, 0)]
    pads[axis] = (1, 0) if low else (0, 1)
    return pads


def face_sum(coupling, axis):
    return jnp.pad(coupling, widths(axis, True)) + jnp.pad(coupling, widths(axis, False))


def net_flow(flow, axis):
    return jnp.pad(flow, widths(axis, False)) - jnp.pad(flow, widths(axis, True))


def coefficients(perm, scale):
    couple_x = scale * harmonic(perm[1:], perm[:-1])
    couple_y = scale * harmonic(perm[:, 1:], perm[:, :-1])
    couple_z = harmonic(perm[:, :, 1:], perm[:, :, :-1])
    diagonal = STORE + face_sum(couple_x, 0) + face_sum(couple_y, 1) + face_sum(couple_z, 2)
    return couple_x, couple_y, couple_z, diagonal


def apply_operator(value, parts):
    couple_x, couple_y, couple_z, diagonal = parts
    flow_x = couple_x * (value[:-1] - value[1:])
    flow_y = couple_y * (value[:, :-1] - value[:, 1:])
    flow_z = couple_z * (value[:, :, :-1] - value[:, :, 1:])
    return STORE * value + net_flow(flow_x, 0) + net_flow(flow_y, 1) + net_flow(flow_z, 2)


def restrict(field):
    sx, sy, sz = field.shape
    return 0.25 * jnp.sum(field.reshape(sx // 2, 2, sy // 2, 2, sz), axis=(1, 3))


def smooth_zero(rhs, parts, sweeps):
    value = OMEGA * rhs / parts[3]
    for step in range(sweeps - 1):
        value = value + OMEGA * (rhs - apply_operator(value, parts)) / parts[3]
    return value


def reference(pressure_init, source, permeability):
    parts0 = coefficients(permeability, 1.0)
    pressure = pressure_init
    for step in range(SWEEPS):
        pressure = pressure + OMEGA * (source - apply_operator(pressure, parts0)) / parts0[3]
    resid0 = source - apply_operator(pressure, parts0)
    rhs_mid = restrict(resid0)
    perm_mid = restrict(permeability)
    parts1 = coefficients(perm_mid, 0.25)
    correction_mid = smooth_zero(rhs_mid, parts1, SWEEPS)
    resid1 = rhs_mid - apply_operator(correction_mid, parts1)
    rhs_coarse = restrict(resid1)
    parts2 = coefficients(restrict(perm_mid), 0.0625)
    correction_coarse = smooth_zero(rhs_coarse, parts2, COARSE)
    return pressure, correction_mid, correction_coarse
```

```python
import jax
import jax.numpy as jnp
from jax import lax
from jax.sharding import PartitionSpec as P

SWEEPS = 2
COARSE = 4

STORE = 0.1
OMEGA = 0.8

FINE_HALO = 8
COARSE_HALO = 4


def harmonic(first, second):
    total = first + second
    return 2.0 * first * second / jnp.where(total > 0, total, 1.0)


def shift(a, axis, step):
    length = a.shape[axis]
    zeros_shape = list(a.shape)
    zeros_shape[axis] = abs(step)
    zeros = jnp.zeros(zeros_shape, a.dtype)
    if step > 0:
        return jnp.concatenate([lax.slice_in_dim(a, step, length, axis=axis), zeros], axis=axis)
    return jnp.concatenate([zeros, lax.slice_in_dim(a, 0, length + step, axis=axis)], axis=axis)


def coefficients(perm, scale):
    couple = []
    for axis in range(3):
        c = harmonic(shift(perm, axis, 1), perm)
        if axis < 2:
            c = scale * c
        couple.append(c)
    diagonal = STORE
    for axis in range(3):
        diagonal = diagonal + (shift(couple[axis], axis, -1) + couple[axis])
    return couple, diagonal


def apply_operator(value, parts):
    couple, diagonal = parts
    out = STORE * value
    for axis in range(3):
        flow = couple[axis] * (value - shift(value, axis, 1))
        out = out + (flow - shift(flow, axis, -1))
    return out


def restrict(field):
    sx, sy, sz = field.shape
    return 0.25 * jnp.sum(field.reshape(sx // 2, 2, sy // 2, 2, sz), axis=(1, 3))


def exchange(x, h):
    nxg = lax.axis_size("gx")
    nyg = lax.axis_size("gy")
    nx, ny = x.shape[-3], x.shape[-2]

    def sl(a, lo, hi, axis):
        return lax.slice_in_dim(a, lo, hi, axis=a.ndim + axis)

    def send(block, dx, dy):
        if dx == 0:
            pairs = [(j, j + dy) for j in range(nyg) if 0 <= j + dy < nyg]
            return lax.ppermute(block, "gy", pairs)
        if dy == 0:
            pairs = [(i, i + dx) for i in range(nxg) if 0 <= i + dx < nxg]
            return lax.ppermute(block, "gx", pairs)
        pairs = [
            (i * nyg + j, (i + dx) * nyg + j + dy)
            for i in range(nxg)
            for j in range(nyg)
            if 0 <= i + dx < nxg and 0 <= j + dy < nyg
        ]
        return lax.ppermute(block, ("gx", "gy"), pairs)

    x_lo = sl(x, 0, h, -3)
    x_hi = sl(x, nx - h, nx, -3)
    y_lo = sl(x, 0, h, -2)
    y_hi = sl(x, ny - h, ny, -2)
    from_xm = send(x_hi, 1, 0)
    from_xp = send(x_lo, -1, 0)
    from_ym = send(y_hi, 0, 1)
    from_yp = send(y_lo, 0, -1)
    from_mm = send(sl(x_hi, ny - h, ny, -2), 1, 1)
    from_mp = send(sl(x_hi, 0, h, -2), 1, -1)
    from_pm = send(sl(x_lo, ny - h, ny, -2), -1, 1)
    from_pp = send(sl(x_lo, 0, h, -2), -1, -1)
    low = jnp.concatenate([from_mm, from_xm, from_mp], axis=-2)
    mid = jnp.concatenate([from_ym, x, from_yp], axis=-2)
    high = jnp.concatenate([from_pm, from_xp, from_pp], axis=-2)
    return jnp.concatenate([low, mid, high], axis=-3)


def inner(a, h):
    return a[h:a.shape[0] - h, h:a.shape[1] - h]


def body(pressure_init, source, permeability):
    h0 = FINE_HALO
    region = exchange(jnp.stack([permeability, pressure_init, source]), h0)
    perm0, pressure, src = region[0], region[1], region[2]
    parts0 = coefficients(perm0, 1.0)
    for step in range(SWEEPS):
        pressure = pressure + OMEGA * (src - apply_operator(pressure, parts0)) / parts0[1]
    resid0 = src - apply_operator(pressure, parts0)
    pressure_out = inner(pressure, h0)

    h1 = h0 // 2
    rhs_mid = restrict(resid0)
    perm_mid = restrict(perm0)
    parts1 = coefficients(perm_mid, 0.25)
    value = OMEGA * rhs_mid / parts1[1]
    for step in range(SWEEPS - 1):
        value = value + OMEGA * (rhs_mid - apply_operator(value, parts1)) / parts1[1]
    resid1 = rhs_mid - apply_operator(value, parts1)
    correction_mid = inner(value, h1)

    h2 = COARSE_HALO
    rhs_coarse = restrict(inner(resid1, h1))
    perm_coarse = restrict(inner(perm_mid, h1))
    region2 = exchange(jnp.stack([perm_coarse, rhs_coarse]), h2)
    perm2, rhs2 = region2[0], region2[1]
    parts2 = coefficients(perm2, 0.0625)
    value = OMEGA * rhs2 / parts2[1]
    for step in range(COARSE - 1):
        value = value + OMEGA * (rhs2 - apply_operator(value, parts2)) / parts2[1]
    correction_coarse = inner(value, h2)
    return (pressure_out, correction_mid, correction_coarse)


def solution(mesh):
    placed = (P("gx", "gy", None), P("gx", "gy", None), P("gx", "gy", None))
    return jax.shard_map(
        body,
        mesh=mesh,
        in_specs=placed,
        out_specs=(P("gx", "gy", None), P("gx", "gy", None), P("gx", "gy", None)),
        check_vma=False,
    )
```

```python
import jax
import jax.numpy as jnp
from jax import lax
from jax.sharding import PartitionSpec as P

SWEEPS = 2
COARSE = 4

STORE = 0.1
OMEGA = 0.8

FINE_HALO = 8
COARSE_HALO = 4


def harmonic(first, second):
    total = first + second
    return 2.0 * first * second / jnp.where(total > 0, total, 1.0)


def shift(a, axis, step):
    length = a.shape[axis]
    zeros_shape = list(a.shape)
    zeros_shape[axis] = abs(step)
    zeros = jnp.zeros(zeros_shape, a.dtype)
    if step > 0:
        return jnp.concatenate([lax.slice_in_dim(a, step, length, axis=axis), zeros], axis=axis)
    return jnp.concatenate([zeros, lax.slice_in_dim(a, 0, length + step, axis=axis)], axis=axis)


def coefficients(perm, scale):
    couple = []
    for axis in range(3):
        c = harmonic(shift(perm, axis, 1), perm)
        if axis < 2:
            c = scale * c
        couple.append(c)
    diagonal = STORE
    for axis in range(3):
        diagonal = diagonal + (shift(couple[axis], axis, -1) + couple[axis])
    return couple, diagonal


def apply_operator(value, parts):
    couple, diagonal = parts
    out = STORE * value
    for axis in range(3):
        flow = couple[axis] * (value - shift(value, axis, 1))
        out = out + (flow - shift(flow, axis, -1))
    return out


def restrict(field):
    sx, sy, sz = field.shape
    return 0.25 * jnp.sum(field.reshape(sx // 2, 2, sy // 2, 2, sz), axis=(1, 3))


def exchange(x, h):
    for axis, dim in (("gx", x.ndim - 3), ("gy", x.ndim - 2)):
        count, length = lax.axis_size(axis), x.shape[dim]
        up = [(i, i + 1) for i in range(count - 1)]
        down = [(i + 1, i) for i in range(count - 1)]
        before = lax.ppermute(lax.slice_in_dim(x, length - h, length, axis=dim), axis, up)
        after = lax.ppermute(lax.slice_in_dim(x, 0, h, axis=dim), axis, down)
        x = jnp.concatenate([before, x, after], axis=dim)
    return x


def inner(a, h):
    return a[h:a.shape[0] - h, h:a.shape[1] - h]


def body(pressure_init, source, permeability):
    h0 = FINE_HALO
    region = exchange(jnp.stack([permeability, pressure_init, source]), h0)
    perm0, pressure, src = region[0], region[1], region[2]
    parts0 = coefficients(perm0, 1.0)
    for step in range(SWEEPS):
        pressure = pressure + OMEGA * (src - apply_operator(pressure, parts0)) / parts0[1]
    resid0 = src - apply_operator(pressure, parts0)
    pressure_out = inner(pressure, h0)

    h1 = h0 // 2
    rhs_mid = restrict(resid0)
    perm_mid = restrict(perm0)
    parts1 = coefficients(perm_mid, 0.25)
    value = OMEGA * rhs_mid / parts1[1]
    for step in range(SWEEPS - 1):
        value = value + OMEGA * (rhs_mid - apply_operator(value, parts1)) / parts1[1]
    resid1 = rhs_mid - apply_operator(value, parts1)
    correction_mid = inner(value, h1)

    h2 = COARSE_HALO
    rhs_coarse = restrict(inner(resid1, h1))
    perm_coarse = restrict(inner(perm_mid, h1))
    region2 = exchange(jnp.stack([perm_coarse, rhs_coarse]), h2)
    perm2, rhs2 = region2[0], region2[1]
    parts2 = coefficients(perm2, 0.0625)
    value = OMEGA * rhs2 / parts2[1]
    for step in range(COARSE - 1):
        value = value + OMEGA * (rhs2 - apply_operator(value, parts2)) / parts2[1]
    correction_coarse = inner(value, h2)
    return (pressure_out, correction_mid, correction_coarse)


def solution(mesh):
    placed = (P("gx", "gy", None), P("gx", "gy", None), P("gx", "gy", None))
    return jax.shard_map(
        body,
        mesh=mesh,
        in_specs=placed,
        out_specs=(P("gx", "gy", None), P("gx", "gy", None), P("gx", "gy", None)),
        check_vma=False,
    )
```

```python
import jax
import jax.numpy as jnp
from jax import lax
from jax.experimental import pallas as pl
from jax.experimental.pallas import tpu as pltpu
from jax.sharding import PartitionSpec as P

SWEEPS = 2
COARSE = 4

STORE = 0.1
OMEGA = 0.8

FINE_HALO = 8
COARSE_HALO = 4


def harmonic(first, second):
    total = first + second
    return 2.0 * first * second / jnp.where(total > 0, total, 1.0)


def shift(a, axis, step):
    length = a.shape[axis]
    zeros_shape = list(a.shape)
    zeros_shape[axis] = abs(step)
    zeros = jnp.zeros(zeros_shape, a.dtype)
    if step > 0:
        return jnp.concatenate([lax.slice_in_dim(a, step, length, axis=axis), zeros], axis=axis)
    return jnp.concatenate([zeros, lax.slice_in_dim(a, 0, length + step, axis=axis)], axis=axis)


def coefficients(perm, scale):
    couple = []
    for axis in range(3):
        c = harmonic(shift(perm, axis, 1), perm)
        if axis < 2:
            c = scale * c
        couple.append(c)
    diagonal = STORE
    for axis in range(3):
        diagonal = diagonal + (shift(couple[axis], axis, -1) + couple[axis])
    return couple, diagonal


def apply_operator(value, parts):
    couple, diagonal = parts
    out = STORE * value
    for axis in range(3):
        flow = couple[axis] * (value - shift(value, axis, 1))
        out = out + (flow - shift(flow, axis, -1))
    return out


def restrict(field):
    sx, sy, sz = field.shape
    return 0.25 * jnp.sum(field.reshape(sx // 2, 2, sy // 2, 2, sz), axis=(1, 3))


def exchange(x, h):
    for axis, dim in (("gx", x.ndim - 3), ("gy", x.ndim - 2)):
        count, length = lax.axis_size(axis), x.shape[dim]
        up = [(i, i + 1) for i in range(count - 1)]
        down = [(i + 1, i) for i in range(count - 1)]
        before = lax.ppermute(lax.slice_in_dim(x, length - h, length, axis=dim), axis, up)
        after = lax.ppermute(lax.slice_in_dim(x, 0, h, axis=dim), axis, down)
        x = jnp.concatenate([before, x, after], axis=dim)
    return x


def inner(a, h):
    return a[h:a.shape[0] - h, h:a.shape[1] - h]


def k_shift(a, axis, step):
    n = a.shape[axis]
    if axis == 0:
        if step > 0:
            return jnp.concatenate([a[step:], a[:step]], axis=0)
        return jnp.concatenate([a[n + step:], a[:n + step]], axis=0)
    return pltpu.roll(a, (-step) % n, axis)


def k_coefficients(perm, scale):
    couple = []
    last_z = lax.broadcasted_iota(jnp.int32, perm.shape, 2) == perm.shape[2] - 1
    for axis in range(3):
        c = harmonic(k_shift(perm, axis, 1), perm)
        if axis < 2:
            c = scale * c
        else:
            c = jnp.where(last_z, 0.0, c)
        couple.append(c)
    diagonal = STORE
    for axis in range(3):
        diagonal = diagonal + (k_shift(couple[axis], axis, -1) + couple[axis])
    return couple, diagonal


def k_apply(value, parts):
    couple, diagonal = parts
    out = STORE * value
    for axis in range(3):
        flow = couple[axis] * (value - k_shift(value, axis, 1))
        out = out + (flow - k_shift(flow, axis, -1))
    return out


def k_restrict(ref, lo, nx, ny):
    def at(dx, dy):
        return ref[pl.ds(lo + dx, nx, stride=2), pl.ds(lo + dy, ny, stride=2), :]
    return 0.25 * ((at(0, 0) + at(1, 0)) + (at(0, 1) + at(1, 1)))


def fine_kernel(region, p_out, mid_out, rhs2_out, perm2_out, k0_scr, r0_scr, k1_scr, r1_scr):
    h0 = FINE_HALO
    h1 = h0 // 2
    perm0 = region[0]
    pressure = region[1]
    src = region[2]
    parts0 = k_coefficients(perm0, 1.0)
    for step in range(SWEEPS):
        pressure = pressure + OMEGA * (src - k_apply(pressure, parts0)) / parts0[1]
    resid0 = src - k_apply(pressure, parts0)
    p_out[...] = inner(pressure, h0)
    k0_scr[...] = perm0
    r0_scr[...] = resid0
    cx, cy = r0_scr.shape[0] // 2, r0_scr.shape[1] // 2
    rhs_mid = k_restrict(r0_scr, 0, cx, cy)
    perm_mid = k_restrict(k0_scr, 0, cx, cy)
    parts1 = k_coefficients(perm_mid, 0.25)
    value = OMEGA * rhs_mid / parts1[1]
    for step in range(SWEEPS - 1):
        value = value + OMEGA * (rhs_mid - k_apply(value, parts1)) / parts1[1]
    resid1 = rhs_mid - k_apply(value, parts1)
    k1_scr[...] = perm_mid
    mx, my = mid_out.shape[0], mid_out.shape[1]
    r1_scr[...] = value
    mid_out[...] = r1_scr[pl.ds(h1, mx), pl.ds(h1, my), :]
    r1_scr[...] = resid1
    rhs2_out[...] = k_restrict(r1_scr, h1, mx // 2, my // 2)
    perm2_out[...] = k_restrict(k1_scr, h1, mx // 2, my // 2)


def coarse_kernel(region, out, scr):
    h2 = COARSE_HALO
    perm2 = region[0]
    rhs2 = region[1]
    parts2 = k_coefficients(perm2, 0.0625)
    value = OMEGA * rhs2 / parts2[1]
    for step in range(COARSE - 1):
        value = value + OMEGA * (rhs2 - k_apply(value, parts2)) / parts2[1]
    scr[...] = value
    out[...] = scr[pl.ds(h2, out.shape[0]), pl.ds(h2, out.shape[1]), :]


def vmem_call(kernel, outs, scratch, *args):
    return pl.pallas_call(
        kernel,
        out_shape=[jax.ShapeDtypeStruct(s, jnp.float32) for s in outs],
        in_specs=[pl.BlockSpec(memory_space=pltpu.VMEM) for a in args],
        out_specs=[pl.BlockSpec(memory_space=pltpu.VMEM) for s in outs],
        scratch_shapes=[pltpu.VMEM(s, jnp.float32) for s in scratch],
        compiler_params=pltpu.CompilerParams(vmem_limit_bytes=48 * 1024 * 1024),
    )(*args)


def body(pressure_init, source, permeability):
    h0, h2 = FINE_HALO, COARSE_HALO
    nx, ny, nz = pressure_init.shape
    region = exchange(jnp.stack([permeability, pressure_init, source]), h0)
    px, py = nx + 2 * h0, ny + 2 * h0
    mid = (nx // 2, ny // 2, nz)
    coarse = (nx // 4, ny // 4, nz)
    pressure_out, correction_mid, rhs_coarse, perm_coarse = vmem_call(
        fine_kernel,
        [(nx, ny, nz), mid, coarse, coarse],
        [(px, py, nz), (px, py, nz), (px // 2, py // 2, nz), (px // 2, py // 2, nz)],
        region,
    )
    region2 = exchange(jnp.stack([perm_coarse, rhs_coarse]), h2)
    c2x, c2y = coarse[0] + 2 * h2, coarse[1] + 2 * h2
    (correction_coarse,) = vmem_call(coarse_kernel, [coarse], [(c2x, c2y, nz)], region2)
    return (pressure_out, correction_mid, correction_coarse)


def solution(mesh):
    placed = (P("gx", "gy", None), P("gx", "gy", None), P("gx", "gy", None))
    return jax.shard_map(
        body,
        mesh=mesh,
        in_specs=placed,
        out_specs=(P("gx", "gy", None), P("gx", "gy", None), P("gx", "gy", None)),
        check_vma=False,
    )
```

```python
import jax
import jax.numpy as jnp
from jax import lax
from jax.experimental import pallas as pl
from jax.experimental.pallas import tpu as pltpu
from jax.sharding import PartitionSpec as P

SWEEPS = 2
COARSE = 4

STORE = 0.1
OMEGA = 0.8

FINE_HALO = 8
COARSE_HALO = 4


def harmonic(first, second):
    total = first + second
    return 2.0 * first * second / jnp.where(total > 0, total, 1.0)


def shift(a, axis, step):
    length = a.shape[axis]
    zeros_shape = list(a.shape)
    zeros_shape[axis] = abs(step)
    zeros = jnp.zeros(zeros_shape, a.dtype)
    if step > 0:
        return jnp.concatenate([lax.slice_in_dim(a, step, length, axis=axis), zeros], axis=axis)
    return jnp.concatenate([zeros, lax.slice_in_dim(a, 0, length + step, axis=axis)], axis=axis)


def coefficients(perm, scale):
    couple = []
    for axis in range(3):
        c = harmonic(shift(perm, axis, 1), perm)
        if axis < 2:
            c = scale * c
        couple.append(c)
    diagonal = STORE
    for axis in range(3):
        diagonal = diagonal + (shift(couple[axis], axis, -1) + couple[axis])
    return couple, diagonal


def apply_operator(value, parts):
    couple, diagonal = parts
    out = STORE * value
    for axis in range(3):
        flow = couple[axis] * (value - shift(value, axis, 1))
        out = out + (flow - shift(flow, axis, -1))
    return out


def restrict(field):
    sx, sy, sz = field.shape
    return 0.25 * jnp.sum(field.reshape(sx // 2, 2, sy // 2, 2, sz), axis=(1, 3))


def exchange(x, h):
    for axis, dim in (("gy", x.ndim - 2), ("gx", x.ndim - 3)):
        count, length = lax.axis_size(axis), x.shape[dim]
        up = [(i, i + 1) for i in range(count - 1)]
        down = [(i + 1, i) for i in range(count - 1)]
        before = lax.ppermute(lax.slice_in_dim(x, length - h, length, axis=dim), axis, up)
        after = lax.ppermute(lax.slice_in_dim(x, 0, h, axis=dim), axis, down)
        x = jnp.concatenate([before, x, after], axis=dim)
    return x


def inner(a, h):
    return a[h:a.shape[0] - h, h:a.shape[1] - h]


def k_shift(a, axis, step):
    n = a.shape[axis]
    if axis == 0:
        if step > 0:
            return jnp.concatenate([a[step:], a[:step]], axis=0)
        return jnp.concatenate([a[n + step:], a[:n + step]], axis=0)
    return pltpu.roll(a, (-step) % n, axis)


def k_coefficients(perm, scale):
    couple = []
    last_z = lax.broadcasted_iota(jnp.int32, perm.shape, 2) == perm.shape[2] - 1
    for axis in range(3):
        c = harmonic(k_shift(perm, axis, 1), perm)
        if axis < 2:
            c = scale * c
        else:
            c = jnp.where(last_z, 0.0, c)
        couple.append(c)
    diagonal = STORE
    for axis in range(3):
        diagonal = diagonal + (k_shift(couple[axis], axis, -1) + couple[axis])
    return couple, diagonal


def k_apply(value, parts):
    couple, diagonal = parts
    out = STORE * value
    for axis in range(3):
        flow = couple[axis] * (value - k_shift(value, axis, 1))
        out = out + (flow - k_shift(flow, axis, -1))
    return out


def k_restrict(ref, lo, nx, ny):
    def at(dx, dy):
        return ref[pl.ds(lo + dx, nx, stride=2), pl.ds(lo + dy, ny, stride=2), :]
    return 0.25 * ((at(0, 0) + at(1, 0)) + (at(0, 1) + at(1, 1)))


def fine_kernel(region, p_out, mid_out, rhs2_out, perm2_out, k0_scr, r0_scr, k1_scr, r1_scr):
    h0 = FINE_HALO
    h1 = h0 // 2
    perm0 = region[0]
    pressure = region[1]
    src = region[2]
    parts0 = k_coefficients(perm0, 1.0)
    for step in range(SWEEPS):
        pressure = pressure + OMEGA * (src - k_apply(pressure, parts0)) / parts0[1]
    resid0 = src - k_apply(pressure, parts0)
    p_out[...] = inner(pressure, h0)
    k0_scr[...] = perm0
    r0_scr[...] = resid0
    cx, cy = r0_scr.shape[0] // 2, r0_scr.shape[1] // 2
    rhs_mid = k_restrict(r0_scr, 0, cx, cy)
    perm_mid = k_restrict(k0_scr, 0, cx, cy)
    parts1 = k_coefficients(perm_mid, 0.25)
    value = OMEGA * rhs_mid / parts1[1]
    for step in range(SWEEPS - 1):
        value = value + OMEGA * (rhs_mid - k_apply(value, parts1)) / parts1[1]
    resid1 = rhs_mid - k_apply(value, parts1)
    k1_scr[...] = perm_mid
    mx, my = mid_out.shape[0], mid_out.shape[1]
    r1_scr[...] = value
    mid_out[...] = r1_scr[pl.ds(h1, mx), pl.ds(h1, my), :]
    r1_scr[...] = resid1
    rhs2_out[...] = k_restrict(r1_scr, h1, mx // 2, my // 2)
    perm2_out[...] = k_restrict(k1_scr, h1, mx // 2, my // 2)


def coarse_kernel(region, out, scr):
    h2 = COARSE_HALO
    perm2 = region[0]
    rhs2 = region[1]
    parts2 = k_coefficients(perm2, 0.0625)
    value = OMEGA * rhs2 / parts2[1]
    for step in range(COARSE - 1):
        value = value + OMEGA * (rhs2 - k_apply(value, parts2)) / parts2[1]
    scr[...] = value
    out[...] = scr[pl.ds(h2, out.shape[0]), pl.ds(h2, out.shape[1]), :]


def vmem_call(kernel, outs, scratch, *args):
    return pl.pallas_call(
        kernel,
        out_shape=[jax.ShapeDtypeStruct(s, jnp.float32) for s in outs],
        in_specs=[pl.BlockSpec(memory_space=pltpu.VMEM) for a in args],
        out_specs=[pl.BlockSpec(memory_space=pltpu.VMEM) for s in outs],
        scratch_shapes=[pltpu.VMEM(s, jnp.float32) for s in scratch],
        compiler_params=pltpu.CompilerParams(vmem_limit_bytes=48 * 1024 * 1024),
    )(*args)


def body(pressure_init, source, permeability):
    h0, h2 = FINE_HALO, COARSE_HALO
    nx, ny, nz = pressure_init.shape
    region = exchange(jnp.stack([permeability, pressure_init, source]), h0)
    px, py = nx + 2 * h0, ny + 2 * h0
    mid = (nx // 2, ny // 2, nz)
    coarse = (nx // 4, ny // 4, nz)
    pressure_out, correction_mid, rhs_coarse, perm_coarse = vmem_call(
        fine_kernel,
        [(nx, ny, nz), mid, coarse, coarse],
        [(px, py, nz), (px, py, nz), (px // 2, py // 2, nz), (px // 2, py // 2, nz)],
        region,
    )
    region2 = exchange(jnp.stack([perm_coarse, rhs_coarse]), h2)
    c2x, c2y = coarse[0] + 2 * h2, coarse[1] + 2 * h2
    (correction_coarse,) = vmem_call(coarse_kernel, [coarse], [(c2x, c2y, nz)], region2)
    return (pressure_out, correction_mid, correction_coarse)


def solution(mesh):
    placed = (P("gx", "gy", None), P("gx", "gy", None), P("gx", "gy", None))
    return jax.shard_map(
        body,
        mesh=mesh,
        in_specs=placed,
        out_specs=(P("gx", "gy", None), P("gx", "gy", None), P("gx", "gy", None)),
        check_vma=False,
    )
```

```python
import jax
import jax.numpy as jnp
from jax import lax
from jax.experimental import pallas as pl
from jax.experimental.pallas import tpu as pltpu
from jax.sharding import PartitionSpec as P

SWEEPS = 2
COARSE = 4

STORE = 0.1
OMEGA = 0.8

FINE_HALO = 8
COARSE_HALO = 4


def harmonic(first, second):
    total = first + second
    return 2.0 * first * second / jnp.where(total > 0, total, 1.0)


def shift(a, axis, step):
    length = a.shape[axis]
    zeros_shape = list(a.shape)
    zeros_shape[axis] = abs(step)
    zeros = jnp.zeros(zeros_shape, a.dtype)
    if step > 0:
        return jnp.concatenate([lax.slice_in_dim(a, step, length, axis=axis), zeros], axis=axis)
    return jnp.concatenate([zeros, lax.slice_in_dim(a, 0, length + step, axis=axis)], axis=axis)


def coefficients(perm, scale):
    couple = []
    for axis in range(3):
        c = harmonic(shift(perm, axis, 1), perm)
        if axis < 2:
            c = scale * c
        couple.append(c)
    diagonal = STORE
    for axis in range(3):
        diagonal = diagonal + (shift(couple[axis], axis, -1) + couple[axis])
    return couple, diagonal


def apply_operator(value, parts):
    couple, diagonal = parts
    out = STORE * value
    for axis in range(3):
        flow = couple[axis] * (value - shift(value, axis, 1))
        out = out + (flow - shift(flow, axis, -1))
    return out


def restrict(field):
    sx, sy, sz = field.shape
    return 0.25 * jnp.sum(field.reshape(sx // 2, 2, sy // 2, 2, sz), axis=(1, 3))


def exchange(tiles, h):
    lo_y, hi_y, lo_x, hi_x = exchange_pieces(tiles, h)
    mid = jnp.concatenate([lo_y, jnp.stack(tiles), hi_y], axis=2)
    return jnp.concatenate([lo_x, mid, hi_x], axis=1)


def shift_in(edge, axis, step):
    count = lax.axis_size(axis)
    pairs = [(i, i + step) for i in range(count) if 0 <= i + step < count]
    return lax.ppermute(edge, axis, pairs)


def exchange_pieces(tiles, h):
    ny = tiles[0].shape[1]
    nx = tiles[0].shape[0]
    lo_y = shift_in(jnp.stack([t[:, ny - h:] for t in tiles]), "gy", 1)
    hi_y = shift_in(jnp.stack([t[:, :h] for t in tiles]), "gy", -1)

    def rows(lo, hi):
        body = jnp.stack([t[lo:hi] for t in tiles])
        return jnp.concatenate([lo_y[:, lo:hi], body, hi_y[:, lo:hi]], axis=2)

    lo_x = shift_in(rows(nx - h, nx), "gx", 1)
    hi_x = shift_in(rows(0, h), "gx", -1)
    return lo_y, hi_y, lo_x, hi_x


def inner(a, h):
    return a[h:a.shape[0] - h, h:a.shape[1] - h]


def k_shift(a, axis, step):
    n = a.shape[axis]
    if axis == 0:
        if step > 0:
            return jnp.concatenate([a[step:], a[:step]], axis=0)
        return jnp.concatenate([a[n + step:], a[:n + step]], axis=0)
    return pltpu.roll(a, (-step) % n, axis)


def k_coefficients(perm, scale):
    couple = []
    last_z = lax.broadcasted_iota(jnp.int32, perm.shape, 2) == perm.shape[2] - 1
    for axis in range(3):
        c = harmonic(k_shift(perm, axis, 1), perm)
        if axis < 2:
            c = scale * c
        else:
            c = jnp.where(last_z, 0.0, c)
        couple.append(c)
    diagonal = STORE
    for axis in range(3):
        diagonal = diagonal + (k_shift(couple[axis], axis, -1) + couple[axis])
    return couple, diagonal


def k_apply(value, parts):
    couple, diagonal = parts
    out = STORE * value
    for axis in range(3):
        flow = couple[axis] * (value - k_shift(value, axis, 1))
        out = out + (flow - k_shift(flow, axis, -1))
    return out


def k_restrict(ref, lo, nx, ny):
    def at(dx, dy):
        return ref[pl.ds(lo + dx, nx, stride=2), pl.ds(lo + dy, ny, stride=2), :]
    return 0.25 * ((at(0, 0) + at(1, 0)) + (at(0, 1) + at(1, 1)))


def fine_kernel(perm_in, p_in, s_in, lo_y, hi_y, lo_x, hi_x,
                p_out, mid_out, rhs2_out, perm2_out, region, k0_scr, r0_scr, k1_scr, r1_scr):
    h0 = FINE_HALO
    h1 = h0 // 2
    nx, ny = perm_in.shape[0], perm_in.shape[1]
    for k, tile in enumerate((perm_in, p_in, s_in)):
        region[k, pl.ds(h0, nx), pl.ds(0, h0), :] = lo_y[k]
        region[k, pl.ds(h0, nx), pl.ds(h0, ny), :] = tile[...]
        region[k, pl.ds(h0, nx), pl.ds(h0 + ny, h0), :] = hi_y[k]
        region[k, pl.ds(0, h0), :, :] = lo_x[k]
        region[k, pl.ds(h0 + nx, h0), :, :] = hi_x[k]
    perm0 = region[0]
    pressure = region[1]
    src = region[2]
    parts0 = k_coefficients(perm0, 1.0)
    for step in range(SWEEPS):
        pressure = pressure + OMEGA * (src - k_apply(pressure, parts0)) / parts0[1]
    resid0 = src - k_apply(pressure, parts0)
    p_out[...] = inner(pressure, h0)
    k0_scr[...] = perm0
    r0_scr[...] = resid0
    cx, cy = r0_scr.shape[0] // 2, r0_scr.shape[1] // 2
    rhs_mid = k_restrict(r0_scr, 0, cx, cy)
    perm_mid = k_restrict(k0_scr, 0, cx, cy)
    parts1 = k_coefficients(perm_mid, 0.25)
    value = OMEGA * rhs_mid / parts1[1]
    for step in range(SWEEPS - 1):
        value = value + OMEGA * (rhs_mid - k_apply(value, parts1)) / parts1[1]
    resid1 = rhs_mid - k_apply(value, parts1)
    k1_scr[...] = perm_mid
    mx, my = mid_out.shape[0], mid_out.shape[1]
    r1_scr[...] = value
    mid_out[...] = r1_scr[pl.ds(h1, mx), pl.ds(h1, my), :]
    r1_scr[...] = resid1
    rhs2_out[...] = k_restrict(r1_scr, h1, mx // 2, my // 2)
    perm2_out[...] = k_restrict(k1_scr, h1, mx // 2, my // 2)


def coarse_kernel(region, out, scr):
    h2 = COARSE_HALO
    perm2 = region[0]
    rhs2 = region[1]
    parts2 = k_coefficients(perm2, 0.0625)
    value = OMEGA * rhs2 / parts2[1]
    for step in range(COARSE - 1):
        value = value + OMEGA * (rhs2 - k_apply(value, parts2)) / parts2[1]
    scr[...] = value
    out[...] = scr[pl.ds(h2, out.shape[0]), pl.ds(h2, out.shape[1]), :]


def vmem_call(kernel, outs, scratch, *args):
    return pl.pallas_call(
        kernel,
        out_shape=[jax.ShapeDtypeStruct(s, jnp.float32) for s in outs],
        in_specs=[pl.BlockSpec(memory_space=pltpu.VMEM) for a in args],
        out_specs=[pl.BlockSpec(memory_space=pltpu.VMEM) for s in outs],
        scratch_shapes=[pltpu.VMEM(s, jnp.float32) for s in scratch],
        compiler_params=pltpu.CompilerParams(vmem_limit_bytes=48 * 1024 * 1024),
    )(*args)


def body(pressure_init, source, permeability):
    h0, h2 = FINE_HALO, COARSE_HALO
    nx, ny, nz = pressure_init.shape
    tiles = [permeability, pressure_init, source]
    pieces = exchange_pieces(tiles, h0)
    px, py = nx + 2 * h0, ny + 2 * h0
    mid = (nx // 2, ny // 2, nz)
    coarse = (nx // 4, ny // 4, nz)
    pressure_out, correction_mid, rhs_coarse, perm_coarse = vmem_call(
        fine_kernel,
        [(nx, ny, nz), mid, coarse, coarse],
        [(3, px, py, nz), (px, py, nz), (px, py, nz), (px // 2, py // 2, nz), (px // 2, py // 2, nz)],
        *tiles,
        *pieces,
    )
    region2 = exchange([perm_coarse, rhs_coarse], h2)
    c2x, c2y = coarse[0] + 2 * h2, coarse[1] + 2 * h2
    (correction_coarse,) = vmem_call(coarse_kernel, [coarse], [(c2x, c2y, nz)], region2)
    return (pressure_out, correction_mid, correction_coarse)


def solution(mesh):
    placed = (P("gx", "gy", None), P("gx", "gy", None), P("gx", "gy", None))
    return jax.shard_map(
        body,
        mesh=mesh,
        in_specs=placed,
        out_specs=(P("gx", "gy", None), P("gx", "gy", None), P("gx", "gy", None)),
        check_vma=False,
    )
```

```python
import jax
import jax.numpy as jnp
from jax import lax
from jax.experimental import pallas as pl
from jax.experimental.pallas import tpu as pltpu
from jax.sharding import PartitionSpec as P

SWEEPS = 2
COARSE = 4

STORE = 0.1
OMEGA = 0.8

FINE_HALO = 8
FINE_Y_HALO = 20
COARSE_HALO = 4


def harmonic(first, second):
    total = first + second
    return 2.0 * first * second / jnp.where(total > 0, total, 1.0)


def shift(a, axis, step):
    length = a.shape[axis]
    zeros_shape = list(a.shape)
    zeros_shape[axis] = abs(step)
    zeros = jnp.zeros(zeros_shape, a.dtype)
    if step > 0:
        return jnp.concatenate([lax.slice_in_dim(a, step, length, axis=axis), zeros], axis=axis)
    return jnp.concatenate([zeros, lax.slice_in_dim(a, 0, length + step, axis=axis)], axis=axis)


def coefficients(perm, scale):
    couple = []
    for axis in range(3):
        c = harmonic(shift(perm, axis, 1), perm)
        if axis < 2:
            c = scale * c
        couple.append(c)
    diagonal = STORE
    for axis in range(3):
        diagonal = diagonal + (shift(couple[axis], axis, -1) + couple[axis])
    return couple, diagonal


def apply_operator(value, parts):
    couple, diagonal = parts
    out = STORE * value
    for axis in range(3):
        flow = couple[axis] * (value - shift(value, axis, 1))
        out = out + (flow - shift(flow, axis, -1))
    return out


def restrict(field):
    sx, sy, sz = field.shape
    return 0.25 * jnp.sum(field.reshape(sx // 2, 2, sy // 2, 2, sz), axis=(1, 3))


def exchange_x(tiles, h):
    nx = tiles[0].shape[0]
    lo_x = shift_in(jnp.stack([t[nx - h:] for t in tiles]), "gx", 1)
    hi_x = shift_in(jnp.stack([t[:h] for t in tiles]), "gx", -1)
    return jnp.concatenate([lo_x, jnp.stack(tiles), hi_x], axis=1)


def shift_in(edge, axis, step):
    count = lax.axis_size(axis)
    pairs = [(i, i + step) for i in range(count) if 0 <= i + step < count]
    return lax.ppermute(edge, axis, pairs)


def exchange_pieces(tiles, h, hy=None):
    hy = h if hy is None else hy
    ny = tiles[0].shape[1]
    nx = tiles[0].shape[0]
    lo_y = shift_in(jnp.stack([t[:, ny - hy:] for t in tiles]), "gy", 1)
    hi_y = shift_in(jnp.stack([t[:, :hy] for t in tiles]), "gy", -1)

    def rows(lo, hi):
        body = jnp.stack([t[lo:hi] for t in tiles])
        return jnp.concatenate([lo_y[:, lo:hi], body, hi_y[:, lo:hi]], axis=2)

    lo_x = shift_in(rows(nx - h, nx), "gx", 1)
    hi_x = shift_in(rows(0, h), "gx", -1)
    return lo_y, hi_y, lo_x, hi_x


def inner(a, h):
    return a[h:a.shape[0] - h, h:a.shape[1] - h]


def k_shift(a, axis, step):
    n = a.shape[axis]
    if axis == 0:
        if step > 0:
            return jnp.concatenate([a[step:], a[:step]], axis=0)
        return jnp.concatenate([a[n + step:], a[:n + step]], axis=0)
    return pltpu.roll(a, (-step) % n, axis)


def k_coefficients(perm, scale):
    couple = []
    last_z = lax.broadcasted_iota(jnp.int32, perm.shape, 2) == perm.shape[2] - 1
    for axis in range(3):
        c = harmonic(k_shift(perm, axis, 1), perm)
        if axis < 2:
            c = scale * c
        else:
            c = jnp.where(last_z, 0.0, c)
        couple.append(c)
    diagonal = STORE
    for axis in range(3):
        diagonal = diagonal + (k_shift(couple[axis], axis, -1) + couple[axis])
    return couple, diagonal


def k_apply(value, parts):
    couple, diagonal = parts
    out = STORE * value
    for axis in range(3):
        flow = couple[axis] * (value - k_shift(value, axis, 1))
        out = out + (flow - k_shift(flow, axis, -1))
    return out


def k_restrict(ref, lox, loy, nx, ny):
    def at(dx, dy):
        return ref[pl.ds(lox + dx, nx, stride=2), pl.ds(loy + dy, ny, stride=2), :]
    return 0.25 * ((at(0, 0) + at(1, 0)) + (at(0, 1) + at(1, 1)))


def fine_kernel(perm_in, p_in, s_in, lo_y, hi_y, lo_x, hi_x,
                p_out, mid_out, rhs2_out, perm2_out, region, k0_scr, r0_scr, k1_scr, r1_scr):
    h0, hy, h2 = FINE_HALO, FINE_Y_HALO, COARSE_HALO
    h1, h1y = h0 // 2, hy // 2
    nx, ny = perm_in.shape[0], perm_in.shape[1]
    for k, tile in enumerate((perm_in, p_in, s_in)):
        region[k, pl.ds(h0, nx), pl.ds(0, hy), :] = lo_y[k]
        region[k, pl.ds(h0, nx), pl.ds(hy, ny), :] = tile[...]
        region[k, pl.ds(h0, nx), pl.ds(hy + ny, hy), :] = hi_y[k]
        region[k, pl.ds(0, h0), :, :] = lo_x[k]
        region[k, pl.ds(h0 + nx, h0), :, :] = hi_x[k]
    perm0 = region[0]
    pressure = region[1]
    src = region[2]
    parts0 = k_coefficients(perm0, 1.0)
    for step in range(SWEEPS):
        pressure = pressure + OMEGA * (src - k_apply(pressure, parts0)) / parts0[1]
    resid0 = src - k_apply(pressure, parts0)
    r0_scr[...] = pressure
    p_out[...] = r0_scr[pl.ds(h0, nx), pl.ds(hy, ny), :]
    k0_scr[...] = perm0
    r0_scr[...] = resid0
    cx, cy = r0_scr.shape[0] // 2, r0_scr.shape[1] // 2
    rhs_mid = k_restrict(r0_scr, 0, 0, cx, cy)
    perm_mid = k_restrict(k0_scr, 0, 0, cx, cy)
    parts1 = k_coefficients(perm_mid, 0.25)
    value = OMEGA * rhs_mid / parts1[1]
    for step in range(SWEEPS - 1):
        value = value + OMEGA * (rhs_mid - k_apply(value, parts1)) / parts1[1]
    resid1 = rhs_mid - k_apply(value, parts1)
    k1_scr[...] = perm_mid
    mx, my = mid_out.shape[0], mid_out.shape[1]
    r1_scr[...] = value
    mid_out[...] = r1_scr[pl.ds(h1, mx), pl.ds(h1y, my), :]
    r1_scr[...] = resid1
    qx, qy = rhs2_out.shape[0], rhs2_out.shape[1]
    rhs2_out[...] = k_restrict(r1_scr, h1, h1y - 2 * h2, qx, qy)
    perm2_out[...] = k_restrict(k1_scr, h1, h1y - 2 * h2, qx, qy)


def coarse_kernel(region, out, scr):
    h2 = COARSE_HALO
    perm2 = region[0]
    rhs2 = region[1]
    parts2 = k_coefficients(perm2, 0.0625)
    value = OMEGA * rhs2 / parts2[1]
    for step in range(COARSE - 1):
        value = value + OMEGA * (rhs2 - k_apply(value, parts2)) / parts2[1]
    scr[...] = value
    out[...] = scr[pl.ds(h2, out.shape[0]), pl.ds(h2, out.shape[1]), :]


def vmem_call(kernel, outs, scratch, *args):
    return pl.pallas_call(
        kernel,
        out_shape=[jax.ShapeDtypeStruct(s, jnp.float32) for s in outs],
        in_specs=[pl.BlockSpec(memory_space=pltpu.VMEM) for a in args],
        out_specs=[pl.BlockSpec(memory_space=pltpu.VMEM) for s in outs],
        scratch_shapes=[pltpu.VMEM(s, jnp.float32) for s in scratch],
        compiler_params=pltpu.CompilerParams(vmem_limit_bytes=48 * 1024 * 1024),
    )(*args)


def body(pressure_init, source, permeability):
    h0, h2 = FINE_HALO, COARSE_HALO
    nx, ny, nz = pressure_init.shape
    hy = FINE_Y_HALO
    tiles = [permeability, pressure_init, source]
    pieces = exchange_pieces(tiles, h0, hy)
    px, py = nx + 2 * h0, ny + 2 * hy
    mid = (nx // 2, ny // 2, nz)
    coarse = (nx // 4, ny // 4, nz)
    coarse_y = (nx // 4, ny // 4 + 2 * h2, nz)
    pressure_out, correction_mid, rhs_coarse, perm_coarse = vmem_call(
        fine_kernel,
        [(nx, ny, nz), mid, coarse_y, coarse_y],
        [(3, px, py, nz), (px, py, nz), (px, py, nz), (px // 2, py // 2, nz), (px // 2, py // 2, nz)],
        *tiles,
        *pieces,
    )
    region2 = exchange_x([perm_coarse, rhs_coarse], h2)
    c2x, c2y = coarse[0] + 2 * h2, coarse[1] + 2 * h2
    (correction_coarse,) = vmem_call(coarse_kernel, [coarse], [(c2x, c2y, nz)], region2)
    return (pressure_out, correction_mid, correction_coarse)


def solution(mesh):
    placed = (P("gx", "gy", None), P("gx", "gy", None), P("gx", "gy", None))
    return jax.shard_map(
        body,
        mesh=mesh,
        in_specs=placed,
        out_specs=(P("gx", "gy", None), P("gx", "gy", None), P("gx", "gy", None)),
        check_vma=False,
    )
```

```python
import jax
import jax.numpy as jnp
from jax import lax
from jax.experimental import pallas as pl
from jax.experimental.pallas import tpu as pltpu
from jax.sharding import PartitionSpec as P

SWEEPS = 2
COARSE = 4

STORE = 0.1
OMEGA = 0.8

FINE_HALO = 7
FINE_Y_HALO = 8
COARSE_HALO = 4


def harmonic(first, second):
    total = first + second
    return 2.0 * first * second / jnp.where(total > 0, total, 1.0)


def shift(a, axis, step):
    length = a.shape[axis]
    zeros_shape = list(a.shape)
    zeros_shape[axis] = abs(step)
    zeros = jnp.zeros(zeros_shape, a.dtype)
    if step > 0:
        return jnp.concatenate([lax.slice_in_dim(a, step, length, axis=axis), zeros], axis=axis)
    return jnp.concatenate([zeros, lax.slice_in_dim(a, 0, length + step, axis=axis)], axis=axis)


def coefficients(perm, scale):
    couple = []
    for axis in range(3):
        c = harmonic(shift(perm, axis, 1), perm)
        if axis < 2:
            c = scale * c
        couple.append(c)
    diagonal = STORE
    for axis in range(3):
        diagonal = diagonal + (shift(couple[axis], axis, -1) + couple[axis])
    return couple, diagonal


def apply_operator(value, parts):
    couple, diagonal = parts
    out = STORE * value
    for axis in range(3):
        flow = couple[axis] * (value - shift(value, axis, 1))
        out = out + (flow - shift(flow, axis, -1))
    return out


def restrict(field):
    sx, sy, sz = field.shape
    return 0.25 * jnp.sum(field.reshape(sx // 2, 2, sy // 2, 2, sz), axis=(1, 3))


def exchange(x, h, hy=None):
    hy = h if hy is None else hy
    for axis, dim, h in (("gx", x.ndim - 3, h), ("gy", x.ndim - 2, hy)):
        count, length = lax.axis_size(axis), x.shape[dim]
        up = [(i, i + 1) for i in range(count - 1)]
        down = [(i + 1, i) for i in range(count - 1)]
        before = lax.ppermute(lax.slice_in_dim(x, length - h, length, axis=dim), axis, up)
        after = lax.ppermute(lax.slice_in_dim(x, 0, h, axis=dim), axis, down)
        x = jnp.concatenate([before, x, after], axis=dim)
    return x


def inner(a, h, hy=None):
    hy = h if hy is None else hy
    return a[h:a.shape[0] - h, hy:a.shape[1] - hy]


def k_shift(a, axis, step):
    n = a.shape[axis]
    if axis == 0:
        if step > 0:
            return jnp.concatenate([a[step:], a[:step]], axis=0)
        return jnp.concatenate([a[n + step:], a[:n + step]], axis=0)
    return pltpu.roll(a, (-step) % n, axis)


def k_coefficients(perm, scale):
    couple = []
    last_z = lax.broadcasted_iota(jnp.int32, perm.shape, 2) == perm.shape[2] - 1
    for axis in range(3):
        c = harmonic(k_shift(perm, axis, 1), perm)
        if axis < 2:
            c = scale * c
        else:
            c = jnp.where(last_z, 0.0, c)
        couple.append(c)
    diagonal = STORE
    for axis in range(3):
        diagonal = diagonal + (k_shift(couple[axis], axis, -1) + couple[axis])
    return couple, diagonal


def k_apply(value, parts):
    couple, diagonal = parts
    out = STORE * value
    for axis in range(3):
        flow = couple[axis] * (value - k_shift(value, axis, 1))
        out = out + (flow - k_shift(flow, axis, -1))
    return out


def k_restrict(ref, lox, loy, nx, ny):
    def at(dx, dy):
        return ref[pl.ds(lox + dx, nx, stride=2), pl.ds(loy + dy, ny, stride=2), :]
    return 0.25 * ((at(0, 0) + at(1, 0)) + (at(0, 1) + at(1, 1)))


def fine_kernel(region, p_out, mid_out, rhs2_out, perm2_out, k0_scr, r0_scr, k1_scr, r1_scr):
    h0, hy = FINE_HALO, FINE_Y_HALO
    h1, h1y = h0 // 2, hy // 2
    ox = h0 % 2
    perm0 = region[0]
    pressure = region[1]
    src = region[2]
    parts0 = k_coefficients(perm0, 1.0)
    for step in range(SWEEPS):
        pressure = pressure + OMEGA * (src - k_apply(pressure, parts0)) / parts0[1]
    resid0 = src - k_apply(pressure, parts0)
    p_out[...] = inner(pressure, h0, hy)
    k0_scr[...] = perm0
    r0_scr[...] = resid0
    cx, cy = k1_scr.shape[0], k1_scr.shape[1]
    rhs_mid = k_restrict(r0_scr, ox, 0, cx, cy)
    perm_mid = k_restrict(k0_scr, ox, 0, cx, cy)
    parts1 = k_coefficients(perm_mid, 0.25)
    value = OMEGA * rhs_mid / parts1[1]
    for step in range(SWEEPS - 1):
        value = value + OMEGA * (rhs_mid - k_apply(value, parts1)) / parts1[1]
    resid1 = rhs_mid - k_apply(value, parts1)
    k1_scr[...] = perm_mid
    mx, my = mid_out.shape[0], mid_out.shape[1]
    r1_scr[...] = value
    mid_out[...] = r1_scr[pl.ds(h1, mx), pl.ds(h1y, my), :]
    r1_scr[...] = resid1
    rhs2_out[...] = k_restrict(r1_scr, h1, h1y, mx // 2, my // 2)
    perm2_out[...] = k_restrict(k1_scr, h1, h1y, mx // 2, my // 2)


def coarse_kernel(region, out, scr):
    h2 = COARSE_HALO
    perm2 = region[0]
    rhs2 = region[1]
    parts2 = k_coefficients(perm2, 0.0625)
    value = OMEGA * rhs2 / parts2[1]
    for step in range(COARSE - 1):
        value = value + OMEGA * (rhs2 - k_apply(value, parts2)) / parts2[1]
    scr[...] = value
    out[...] = scr[pl.ds(h2, out.shape[0]), pl.ds(h2, out.shape[1]), :]


def vmem_call(kernel, outs, scratch, *args):
    return pl.pallas_call(
        kernel,
        out_shape=[jax.ShapeDtypeStruct(s, jnp.float32) for s in outs],
        in_specs=[pl.BlockSpec(memory_space=pltpu.VMEM) for a in args],
        out_specs=[pl.BlockSpec(memory_space=pltpu.VMEM) for s in outs],
        scratch_shapes=[pltpu.VMEM(s, jnp.float32) for s in scratch],
        compiler_params=pltpu.CompilerParams(vmem_limit_bytes=48 * 1024 * 1024),
    )(*args)


def body(pressure_init, source, permeability):
    h0, h2 = FINE_HALO, COARSE_HALO
    nx, ny, nz = pressure_init.shape
    hy = FINE_Y_HALO
    region = exchange(jnp.stack([permeability, pressure_init, source]), h0, hy)
    px, py = nx + 2 * h0, ny + 2 * hy
    qx = (px - h0 % 2) // 2
    mid = (nx // 2, ny // 2, nz)
    coarse = (nx // 4, ny // 4, nz)
    pressure_out, correction_mid, rhs_coarse, perm_coarse = vmem_call(
        fine_kernel,
        [(nx, ny, nz), mid, coarse, coarse],
        [(px, py, nz), (px, py, nz), (qx, py // 2, nz), (qx, py // 2, nz)],
        region,
    )
    region2 = exchange(jnp.stack([perm_coarse, rhs_coarse]), h2)
    c2x, c2y = coarse[0] + 2 * h2, coarse[1] + 2 * h2
    (correction_coarse,) = vmem_call(coarse_kernel, [coarse], [(c2x, c2y, nz)], region2)
    return (pressure_out, correction_mid, correction_coarse)


def solution(mesh):
    placed = (P("gx", "gy", None), P("gx", "gy", None), P("gx", "gy", None))
    return jax.shard_map(
        body,
        mesh=mesh,
        in_specs=placed,
        out_specs=(P("gx", "gy", None), P("gx", "gy", None), P("gx", "gy", None)),
        check_vma=False,
    )
```

```python
import jax
import jax.numpy as jnp
from jax import lax
from jax.experimental import pallas as pl
from jax.experimental.pallas import tpu as pltpu
from jax.sharding import PartitionSpec as P

SWEEPS = 2
COARSE = 4

STORE = 0.1
OMEGA = 0.8

FINE_HALO = 7
FINE_Y_HALO = 8
COARSE_HALO = 4


def harmonic(first, second):
    total = first + second
    return 2.0 * first * second / jnp.where(total > 0, total, 1.0)


def shift(a, axis, step):
    length = a.shape[axis]
    zeros_shape = list(a.shape)
    zeros_shape[axis] = abs(step)
    zeros = jnp.zeros(zeros_shape, a.dtype)
    if step > 0:
        return jnp.concatenate([lax.slice_in_dim(a, step, length, axis=axis), zeros], axis=axis)
    return jnp.concatenate([zeros, lax.slice_in_dim(a, 0, length + step, axis=axis)], axis=axis)


def coefficients(perm, scale):
    couple = []
    for axis in range(3):
        c = harmonic(shift(perm, axis, 1), perm)
        if axis < 2:
            c = scale * c
        couple.append(c)
    diagonal = STORE
    for axis in range(3):
        diagonal = diagonal + (shift(couple[axis], axis, -1) + couple[axis])
    return couple, diagonal


def apply_operator(value, parts):
    couple, diagonal = parts
    out = STORE * value
    for axis in range(3):
        flow = couple[axis] * (value - shift(value, axis, 1))
        out = out + (flow - shift(flow, axis, -1))
    return out


def restrict(field):
    sx, sy, sz = field.shape
    return 0.25 * jnp.sum(field.reshape(sx // 2, 2, sy // 2, 2, sz), axis=(1, 3))


def exchange(x, h, hy=None):
    hy = h if hy is None else hy
    for axis, dim, h in (("gx", x.ndim - 3, h), ("gy", x.ndim - 2, hy)):
        count, length = lax.axis_size(axis), x.shape[dim]
        up = [(i, i + 1) for i in range(count - 1)]
        down = [(i + 1, i) for i in range(count - 1)]
        before = lax.ppermute(lax.slice_in_dim(x, length - h, length, axis=dim), axis, up)
        after = lax.ppermute(lax.slice_in_dim(x, 0, h, axis=dim), axis, down)
        x = jnp.concatenate([before, x, after], axis=dim)
    return x


def shift_in(edge, axis, step):
    count = lax.axis_size(axis)
    pairs = [(i, i + step) for i in range(count) if 0 <= i + step < count]
    return lax.ppermute(edge, axis, pairs)


def exchange_pieces(tiles, hx, hy):
    nx, ny = tiles[0].shape[0], tiles[0].shape[1]
    lo_x = shift_in(jnp.stack([t[nx - hx:] for t in tiles]), "gx", 1)
    hi_x = shift_in(jnp.stack([t[:hx] for t in tiles]), "gx", -1)

    def cols(lo, hi):
        body = jnp.stack([t[:, lo:hi] for t in tiles])
        return jnp.concatenate([lo_x[:, :, lo:hi], body, hi_x[:, :, lo:hi]], axis=1)

    lo_y = shift_in(cols(ny - hy, ny), "gy", 1)
    hi_y = shift_in(cols(0, hy), "gy", -1)
    return lo_x, hi_x, lo_y, hi_y


def inner(a, h, hy=None):
    hy = h if hy is None else hy
    return a[h:a.shape[0] - h, hy:a.shape[1] - hy]


def k_shift(a, axis, step):
    n = a.shape[axis]
    if axis == 0:
        if step > 0:
            return jnp.concatenate([a[step:], a[:step]], axis=0)
        return jnp.concatenate([a[n + step:], a[:n + step]], axis=0)
    return pltpu.roll(a, (-step) % n, axis)


def k_coefficients(perm, scale):
    couple = []
    last_z = lax.broadcasted_iota(jnp.int32, perm.shape, 2) == perm.shape[2] - 1
    for axis in range(3):
        c = harmonic(k_shift(perm, axis, 1), perm)
        if axis < 2:
            c = scale * c
        else:
            c = jnp.where(last_z, 0.0, c)
        couple.append(c)
    diagonal = STORE
    for axis in range(3):
        diagonal = diagonal + (k_shift(couple[axis], axis, -1) + couple[axis])
    return couple, diagonal


def k_apply(value, parts):
    couple, diagonal = parts
    out = STORE * value
    for axis in range(3):
        flow = couple[axis] * (value - k_shift(value, axis, 1))
        out = out + (flow - k_shift(flow, axis, -1))
    return out


def k_restrict(ref, lox, loy, nx, ny):
    def at(dx, dy):
        return ref[pl.ds(lox + dx, nx, stride=2), pl.ds(loy + dy, ny, stride=2), :]
    return 0.25 * ((at(0, 0) + at(1, 0)) + (at(0, 1) + at(1, 1)))


def fine_kernel(perm_in, p_in, s_in, lo_x, hi_x, lo_y, hi_y,
                p_out, mid_out, rhs2_out, perm2_out, region, k0_scr, r0_scr, k1_scr, r1_scr):
    h0, hy = FINE_HALO, FINE_Y_HALO
    h1, h1y = h0 // 2, hy // 2
    ox = h0 % 2
    nx, ny = perm_in.shape[0], perm_in.shape[1]
    for k, tile in enumerate((perm_in, p_in, s_in)):
        region[k, pl.ds(0, h0), pl.ds(hy, ny), :] = lo_x[k]
        region[k, pl.ds(h0, nx), pl.ds(hy, ny), :] = tile[...]
        region[k, pl.ds(h0 + nx, h0), pl.ds(hy, ny), :] = hi_x[k]
        region[k, :, pl.ds(0, hy), :] = lo_y[k]
        region[k, :, pl.ds(hy + ny, hy), :] = hi_y[k]
    perm0 = region[0]
    pressure = region[1]
    src = region[2]
    parts0 = k_coefficients(perm0, 1.0)
    for step in range(SWEEPS):
        pressure = pressure + OMEGA * (src - k_apply(pressure, parts0)) / parts0[1]
    resid0 = src - k_apply(pressure, parts0)
    p_out[...] = inner(pressure, h0, hy)
    k0_scr[...] = perm0
    r0_scr[...] = resid0
    cx, cy = k1_scr.shape[0], k1_scr.shape[1]
    rhs_mid = k_restrict(r0_scr, ox, 0, cx, cy)
    perm_mid = k_restrict(k0_scr, ox, 0, cx, cy)
    parts1 = k_coefficients(perm_mid, 0.25)
    value = OMEGA * rhs_mid / parts1[1]
    for step in range(SWEEPS - 1):
        value = value + OMEGA * (rhs_mid - k_apply(value, parts1)) / parts1[1]
    resid1 = rhs_mid - k_apply(value, parts1)
    k1_scr[...] = perm_mid
    mx, my = mid_out.shape[0], mid_out.shape[1]
    r1_scr[...] = value
    mid_out[...] = r1_scr[pl.ds(h1, mx), pl.ds(h1y, my), :]
    r1_scr[...] = resid1
    rhs2_out[...] = k_restrict(r1_scr, h1, h1y, mx // 2, my // 2)
    perm2_out[...] = k_restrict(k1_scr, h1, h1y, mx // 2, my // 2)


def coarse_kernel(region, out, scr):
    h2 = COARSE_HALO
    perm2 = region[0]
    rhs2 = region[1]
    parts2 = k_coefficients(perm2, 0.0625)
    value = OMEGA * rhs2 / parts2[1]
    for step in range(COARSE - 1):
        value = value + OMEGA * (rhs2 - k_apply(value, parts2)) / parts2[1]
    scr[...] = value
    out[...] = scr[pl.ds(h2, out.shape[0]), pl.ds(h2, out.shape[1]), :]


def vmem_call(kernel, outs, scratch, *args):
    return pl.pallas_call(
        kernel,
        out_shape=[jax.ShapeDtypeStruct(s, jnp.float32) for s in outs],
        in_specs=[pl.BlockSpec(memory_space=pltpu.VMEM) for a in args],
        out_specs=[pl.BlockSpec(memory_space=pltpu.VMEM) for s in outs],
        scratch_shapes=[pltpu.VMEM(s, jnp.float32) for s in scratch],
        compiler_params=pltpu.CompilerParams(vmem_limit_bytes=48 * 1024 * 1024),
    )(*args)


def body(pressure_init, source, permeability):
    h0, h2 = FINE_HALO, COARSE_HALO
    nx, ny, nz = pressure_init.shape
    hy = FINE_Y_HALO
    tiles = [permeability, pressure_init, source]
    pieces = exchange_pieces(tiles, h0, hy)
    px, py = nx + 2 * h0, ny + 2 * hy
    qx = (px - h0 % 2) // 2
    mid = (nx // 2, ny // 2, nz)
    coarse = (nx // 4, ny // 4, nz)
    pressure_out, correction_mid, rhs_coarse, perm_coarse = vmem_call(
        fine_kernel,
        [(nx, ny, nz), mid, coarse, coarse],
        [(3, px, py, nz), (px, py, nz), (px, py, nz), (qx, py // 2, nz), (qx, py // 2, nz)],
        *tiles,
        *pieces,
    )
    region2 = exchange(jnp.stack([perm_coarse, rhs_coarse]), h2)
    c2x, c2y = coarse[0] + 2 * h2, coarse[1] + 2 * h2
    (correction_coarse,) = vmem_call(coarse_kernel, [coarse], [(c2x, c2y, nz)], region2)
    return (pressure_out, correction_mid, correction_coarse)


def solution(mesh):
    placed = (P("gx", "gy", None), P("gx", "gy", None), P("gx", "gy", None))
    return jax.shard_map(
        body,
        mesh=mesh,
        in_specs=placed,
        out_specs=(P("gx", "gy", None), P("gx", "gy", None), P("gx", "gy", None)),
        check_vma=False,
    )
```

```python
import jax
import jax.numpy as jnp
from jax import lax
from jax.experimental import pallas as pl
from jax.experimental.pallas import tpu as pltpu
from jax.sharding import PartitionSpec as P

SWEEPS = 2
COARSE = 4

STORE = 0.1
OMEGA = 0.8

FINE_HALO = 7
FINE_Y_HALO = 8
COARSE_HALO = 4


def harmonic(first, second):
    total = first + second
    return 2.0 * first * second / jnp.where(total > 0, total, 1.0)


def shift(a, axis, step):
    length = a.shape[axis]
    zeros_shape = list(a.shape)
    zeros_shape[axis] = abs(step)
    zeros = jnp.zeros(zeros_shape, a.dtype)
    if step > 0:
        return jnp.concatenate([lax.slice_in_dim(a, step, length, axis=axis), zeros], axis=axis)
    return jnp.concatenate([zeros, lax.slice_in_dim(a, 0, length + step, axis=axis)], axis=axis)


def coefficients(perm, scale):
    couple = []
    for axis in range(3):
        c = harmonic(shift(perm, axis, 1), perm)
        if axis < 2:
            c = scale * c
        couple.append(c)
    diagonal = STORE
    for axis in range(3):
        diagonal = diagonal + (shift(couple[axis], axis, -1) + couple[axis])
    return couple, diagonal


def apply_operator(value, parts):
    couple, diagonal = parts
    out = STORE * value
    for axis in range(3):
        flow = couple[axis] * (value - shift(value, axis, 1))
        out = out + (flow - shift(flow, axis, -1))
    return out


def restrict(field):
    sx, sy, sz = field.shape
    return 0.25 * jnp.sum(field.reshape(sx // 2, 2, sy // 2, 2, sz), axis=(1, 3))


def exchange(x, h, hy=None):
    hy = h if hy is None else hy
    for axis, dim, h in (("gx", x.ndim - 3, h), ("gy", x.ndim - 2, hy)):
        count, length = lax.axis_size(axis), x.shape[dim]
        up = [(i, i + 1) for i in range(count - 1)]
        down = [(i + 1, i) for i in range(count - 1)]
        before = lax.ppermute(lax.slice_in_dim(x, length - h, length, axis=dim), axis, up)
        after = lax.ppermute(lax.slice_in_dim(x, 0, h, axis=dim), axis, down)
        x = jnp.concatenate([before, x, after], axis=dim)
    return x


def shift_in(edge, axis, step):
    count = lax.axis_size(axis)
    pairs = [(i, i + step) for i in range(count) if 0 <= i + step < count]
    return lax.ppermute(edge, axis, pairs)


def exchange_pieces(tiles, hx, hy):
    nx, ny = tiles[0].shape[0], tiles[0].shape[1]
    lo_x = shift_in(jnp.stack([t[nx - hx:] for t in tiles]), "gx", 1)
    hi_x = shift_in(jnp.stack([t[:hx] for t in tiles]), "gx", -1)

    def cols(lo, hi):
        body = jnp.stack([t[:, lo:hi] for t in tiles])
        return jnp.concatenate([lo_x[:, :, lo:hi], body, hi_x[:, :, lo:hi]], axis=1)

    lo_y = shift_in(cols(ny - hy, ny), "gy", 1)
    hi_y = shift_in(cols(0, hy), "gy", -1)
    return lo_x, hi_x, lo_y, hi_y


def inner(a, h, hy=None):
    hy = h if hy is None else hy
    return a[h:a.shape[0] - h, hy:a.shape[1] - hy]


def k_shift(a, axis, step):
    n = a.shape[axis]
    if axis == 0:
        if step > 0:
            return jnp.concatenate([a[step:], a[:step]], axis=0)
        return jnp.concatenate([a[n + step:], a[:n + step]], axis=0)
    return pltpu.roll(a, (-step) % n, axis)


def k_coefficients(perm, scale):
    couple = []
    last_z = lax.broadcasted_iota(jnp.int32, perm.shape, 2) == perm.shape[2] - 1
    for axis in range(3):
        c = harmonic(k_shift(perm, axis, 1), perm)
        if axis < 2:
            c = scale * c
        else:
            c = jnp.where(last_z, 0.0, c)
        couple.append(c)
    diagonal = STORE
    for axis in range(3):
        diagonal = diagonal + (k_shift(couple[axis], axis, -1) + couple[axis])
    return couple, diagonal


def k_apply(value, parts):
    couple, diagonal = parts
    out = STORE * value
    for axis in range(3):
        flow = couple[axis] * (value - k_shift(value, axis, 1))
        out = out + (flow - k_shift(flow, axis, -1))
    return out


def k_restrict(ref, lox, loy, nx, ny):
    def at(dx, dy):
        return ref[pl.ds(lox + dx, nx, stride=2), pl.ds(loy + dy, ny, stride=2), :]
    return 0.25 * ((at(0, 0) + at(1, 0)) + (at(0, 1) + at(1, 1)))


def fine_kernel(perm_in, p_in, s_in, lo_x, hi_x, lo_y, hi_y,
                p_out, mid_out, rhs2_out, perm2_out, region, k0_scr, r0_scr, k1_scr, r1_scr):
    h0, hy = FINE_HALO, FINE_Y_HALO
    h1, h1y = h0 // 2, hy // 2
    ox = h0 % 2
    nx, ny = perm_in.shape[0], perm_in.shape[1]
    for k, tile in enumerate((perm_in, p_in, s_in)):
        region[k, pl.ds(0, h0), pl.ds(hy, ny), :] = lo_x[k]
        region[k, pl.ds(h0, nx), pl.ds(hy, ny), :] = tile[...]
        region[k, pl.ds(h0 + nx, h0), pl.ds(hy, ny), :] = hi_x[k]
        region[k, :, pl.ds(0, hy), :] = lo_y[k]
        region[k, :, pl.ds(hy + ny, hy), :] = hi_y[k]
    perm0 = region[0]
    pressure = region[1]
    src = region[2]
    parts0 = k_coefficients(perm0, 1.0)
    scale0 = OMEGA / parts0[1]
    for step in range(SWEEPS):
        pressure = pressure + (src - k_apply(pressure, parts0)) * scale0
    resid0 = src - k_apply(pressure, parts0)
    p_out[...] = inner(pressure, h0, hy)
    k0_scr[...] = perm0
    r0_scr[...] = resid0
    cx, cy = k1_scr.shape[0], k1_scr.shape[1]
    rhs_mid = k_restrict(r0_scr, ox, 0, cx, cy)
    perm_mid = k_restrict(k0_scr, ox, 0, cx, cy)
    parts1 = k_coefficients(perm_mid, 0.25)
    scale1 = OMEGA / parts1[1]
    value = rhs_mid * scale1
    for step in range(SWEEPS - 1):
        value = value + (rhs_mid - k_apply(value, parts1)) * scale1
    resid1 = rhs_mid - k_apply(value, parts1)
    k1_scr[...] = perm_mid
    mx, my = mid_out.shape[0], mid_out.shape[1]
    r1_scr[...] = value
    mid_out[...] = r1_scr[pl.ds(h1, mx), pl.ds(h1y, my), :]
    r1_scr[...] = resid1
    rhs2_out[...] = k_restrict(r1_scr, h1, h1y, mx // 2, my // 2)
    perm2_out[...] = k_restrict(k1_scr, h1, h1y, mx // 2, my // 2)


def coarse_kernel(region, out, scr):
    h2 = COARSE_HALO
    perm2 = region[0]
    rhs2 = region[1]
    parts2 = k_coefficients(perm2, 0.0625)
    scale2 = OMEGA / parts2[1]
    value = rhs2 * scale2
    for step in range(COARSE - 1):
        value = value + (rhs2 - k_apply(value, parts2)) * scale2
    scr[...] = value
    out[...] = scr[pl.ds(h2, out.shape[0]), pl.ds(h2, out.shape[1]), :]


def vmem_call(kernel, outs, scratch, *args):
    return pl.pallas_call(
        kernel,
        out_shape=[jax.ShapeDtypeStruct(s, jnp.float32) for s in outs],
        in_specs=[pl.BlockSpec(memory_space=pltpu.VMEM) for a in args],
        out_specs=[pl.BlockSpec(memory_space=pltpu.VMEM) for s in outs],
        scratch_shapes=[pltpu.VMEM(s, jnp.float32) for s in scratch],
        compiler_params=pltpu.CompilerParams(vmem_limit_bytes=48 * 1024 * 1024),
    )(*args)


def body(pressure_init, source, permeability):
    h0, h2 = FINE_HALO, COARSE_HALO
    nx, ny, nz = pressure_init.shape
    hy = FINE_Y_HALO
    tiles = [permeability, pressure_init, source]
    pieces = exchange_pieces(tiles, h0, hy)
    px, py = nx + 2 * h0, ny + 2 * hy
    qx = (px - h0 % 2) // 2
    mid = (nx // 2, ny // 2, nz)
    coarse = (nx // 4, ny // 4, nz)
    pressure_out, correction_mid, rhs_coarse, perm_coarse = vmem_call(
        fine_kernel,
        [(nx, ny, nz), mid, coarse, coarse],
        [(3, px, py, nz), (px, py, nz), (px, py, nz), (qx, py // 2, nz), (qx, py // 2, nz)],
        *tiles,
        *pieces,
    )
    region2 = exchange(jnp.stack([perm_coarse, rhs_coarse]), h2)
    c2x, c2y = coarse[0] + 2 * h2, coarse[1] + 2 * h2
    (correction_coarse,) = vmem_call(coarse_kernel, [coarse], [(c2x, c2y, nz)], region2)
    return (pressure_out, correction_mid, correction_coarse)


def solution(mesh):
    placed = (P("gx", "gy", None), P("gx", "gy", None), P("gx", "gy", None))
    return jax.shard_map(
        body,
        mesh=mesh,
        in_specs=placed,
        out_specs=(P("gx", "gy", None), P("gx", "gy", None), P("gx", "gy", None)),
        check_vma=False,
    )
```
